512 devices in a mesh: wide: 128 (over z, x, core), narrow: 4 (over y).
Axes of the slice: x: 4, y: 4, z: 16, core: 2. Of those that a mesh axis runs over, the one named last changes fastest.
Arguments:
- record: float32 [128, 128, 64, 128], P('wide', 'narrow'), may hold values from -6 to 6
Outputs:
- spectrum: float32 [2, 128, 4, 32, 64, 128], P(None, 'wide', 'narrow')
The draws below stay inside these ranges and needn't reach their ends.
All inputs are finite; a program needn't handle non-finite values.
Results may differ from the reference program's by a relative error of at most 0.00007.
Values sent between devices are 32-bit elements; how exact they have to be, the bound alone decides.
No kernel may reach another device: no remote copies, remote signals or barrier semaphores. Data moves between devices by JAX's collectives and lax.ppermute only.
A program may use at most 64 MiB of HBM per device.

```python
import jax
import jax.numpy as jnp
import numpy as np

F_A = 128
F_B = 128
F_C = 64
F_D = 128
N_NARROW = 4


def block_levels(stream_key, dims, split, low, largest):
    def one(axis_at, parts):
        heights = jax.random.uniform(jax.random.fold_in(jax.random.fold_in(stream_key, 6), axis_at), (parts,), jnp.float32, low / len(split), largest / len(split))
        return jnp.repeat(jnp.exp(heights), dims[axis_at] // parts).reshape((-1,) + (1,) * (len(dims) - axis_at - 1))

    level = one(*split[0])
    for cut in split[1:]:
        level = level * one(*cut)
    return level


def scatter_about(own_key, extent, spread, limit, pieces=(), kind=jnp.bfloat16):
    array = jax.random.normal(own_key, extent, jnp.float32) * spread
    if len(pieces) > 0:
        array = block_levels(own_key, extent, pieces, -0.22, 0.18) * array
    return jnp.clip(array, min=-limit, max=limit).astype(kind)


def setup_inputs(seed: int = 0) -> dict:
    arg_keys = jax.random.split(jax.random.key(seed), 2)
    return {
        "record": scatter_about(arg_keys[0], (F_A, F_B, F_C, F_D), 1.0, 6.0, ((0, 128), (1, 4)), jnp.float32),
    }


def reversed_digits(number, bit_count):
    result = 0 * number
    for position in range(bit_count):
        result = result + ((number // (1 << position)) % 2) * (1 << (bit_count - 1 - position))
    return result


def reference(record):
    spectrum = jnp.fft.fft(record.reshape(-1), norm="ortho")
    levels = N_NARROW.bit_length() - 1
    local_b = F_B // N_NARROW
    residue_order = jnp.asarray(reversed_digits(np.arange(N_NARROW), levels), dtype=jnp.int32)
    halves = []
    for component in (jnp.real(spectrum), jnp.imag(spectrum)):
        arranged = component.reshape(F_D, F_C, local_b, N_NARROW, F_A)
        arranged = jnp.take(arranged, residue_order, axis=3)
        halves.append(jnp.transpose(arranged, (4, 3, 2, 1, 0)))
    return jnp.stack(halves)
```

```python
import math

import jax
import jax.numpy as jnp
from jax import lax
from jax.sharding import PartitionSpec as P

PRECISE = lax.Precision.HIGHEST
TWO_PI = 2.0 * math.pi
DEVICES = ("wide", "narrow")


def reversed_digits(number, bit_count):
    result = 0 * number
    for position in range(bit_count):
        result = result + number // (1 << position) % 2 * (1 << bit_count - 1 - position)
    return result


def unit_turn(phases, length):
    angles = phases.astype(jnp.float32) * (TWO_PI / length)
    return jnp.cos(angles), jnp.sin(angles)


def rotate(values, phases, length):
    cosine, sines = unit_turn(phases, length)
    return jnp.stack(
        [values[0] * cosine + values[1] * sines, values[1] * cosine - values[0] * sines]
    )


def block_table(inputs, outputs, length, factor):
    cosine, sines = unit_turn(inputs[:, None] * outputs[None, :] % length, length)
    cosine = cosine * factor
    sines = sines * factor
    return jnp.stack([jnp.stack([cosine, sines]), jnp.stack([-sines, cosine])])


def shards(record):
    local_a, local_b, size_c, size_d = record.shape
    wide_size = lax.axis_size("wide")
    narrow_size = lax.axis_size("narrow")
    levels = narrow_size.bit_length() - 1
    size_a = local_a * wide_size
    size_b = local_b * narrow_size
    total_count = size_a * size_b * size_c * size_d
    groups = wide_size * narrow_size
    column_count = local_b * size_c * size_d
    columns = column_count // groups
    here = lax.axis_index(DEVICES)

    gathered = lax.all_to_all(
        record.reshape(groups, columns), DEVICES, split_axis=0, concat_axis=0, tiled=True
    )
    slots = jnp.arange(groups, dtype=jnp.int32)
    frequency = slots // narrow_size + size_a * reversed_digits(slots % narrow_size, levels)
    sources = jnp.arange(groups, dtype=jnp.int32)
    table = block_table(sources, frequency, groups, 1.0 / math.sqrt(total_count))[:, 0]
    section = jnp.einsum("pak,an->pkn", table, gathered, precision=PRECISE)
    column_index = here * columns + jnp.arange(columns, dtype=jnp.int32)
    section = rotate(section, frequency[:, None] * column_index[None, :] % total_count, total_count)
    owned = lax.all_to_all(section, DEVICES, split_axis=1, concat_axis=1, tiled=True)
    values = owned.reshape(2, local_b, size_c * size_d)

    index_b = jnp.arange(local_b, dtype=jnp.int32)
    table_b = block_table(index_b, index_b, local_b, 1.0)
    values = jnp.einsum("pqlm,qle->pme", table_b, values, precision=PRECISE)
    inner = jnp.arange(size_c * size_d, dtype=jnp.int32)
    values = rotate(values, index_b[:, None] * inner[None, :] % column_count, column_count)
    values = values.reshape(2, local_b, size_c, size_d)
    index_c = jnp.arange(size_c, dtype=jnp.int32)
    table_c = block_table(index_c, index_c, size_c, 1.0)
    values = jnp.einsum("pqck,qmcd->pmkd", table_c, values, precision=PRECISE)
    index_d = jnp.arange(size_d, dtype=jnp.int32)
    values = rotate(
        values, (index_c[:, None] * index_d[None, :] % (size_c * size_d))[None], size_c * size_d
    )
    table_d = block_table(index_d, index_d, size_d, 1.0)
    values = jnp.einsum("pqdk,qmcd->pmck", table_d, values, precision=PRECISE)
    return values.reshape(2, 1, 1, local_b, size_c, size_d)


def solution(mesh):
    return jax.shard_map(
        shards,
        mesh=mesh,
        in_specs=(P("wide", "narrow", None, None),),
        out_specs=P(None, "wide", "narrow", None, None, None),
        check_vma=False,
    )
```

```python
import math

import jax
import jax.numpy as jnp
from jax import lax
from jax.sharding import PartitionSpec as P

PRECISE = lax.Precision.HIGHEST
TWO_PI = 2.0 * math.pi
DEVICES = ("wide", "narrow")


def reversed_digits(number, bit_count):
    result = 0 * number
    for position in range(bit_count):
        result = result + number // (1 << position) % 2 * (1 << bit_count - 1 - position)
    return result


def unit_turn(phases, length):
    angles = phases.astype(jnp.float32) * (TWO_PI / length)
    return jnp.cos(angles), jnp.sin(angles)


def rotate(values, phases, length):
    cosine, sines = unit_turn(phases, length)
    return jnp.stack(
        [values[0] * cosine + values[1] * sines, values[1] * cosine - values[0] * sines]
    )


def block_table(inputs, outputs, length, factor):
    cosine, sines = unit_turn(inputs[:, None] * outputs[None, :] % length, length)
    cosine = cosine * factor
    sines = sines * factor
    return jnp.stack([jnp.stack([cosine, sines]), jnp.stack([-sines, cosine])])


def shards(record):
    local_a, local_b, size_c, size_d = record.shape
    wide_size = lax.axis_size("wide")
    narrow_size = lax.axis_size("narrow")
    levels = narrow_size.bit_length() - 1
    size_a = local_a * wide_size
    size_b = local_b * narrow_size
    total_count = size_a * size_b * size_c * size_d
    groups = wide_size * narrow_size
    column_count = local_b * size_c * size_d
    columns = column_count // groups
    here = lax.axis_index(DEVICES)

    gathered = lax.all_to_all(
        record.reshape(groups, columns), DEVICES, split_axis=0, concat_axis=0, tiled=True
    )
    slots = jnp.arange(groups, dtype=jnp.int32)
    frequency = slots // narrow_size + size_a * reversed_digits(slots % narrow_size, levels)
    sources = jnp.arange(groups, dtype=jnp.int32)
    table = block_table(sources, frequency, groups, 1.0 / math.sqrt(total_count))[:, 0]
    section = jnp.einsum("pak,an->pkn", table, gathered, precision=PRECISE)
    column_index = here * columns + jnp.arange(columns, dtype=jnp.int32)
    section = rotate(section, frequency[:, None] * column_index[None, :] % total_count, total_count)
    section = jnp.transpose(section, (1, 0, 2))
    owned = lax.all_to_all(section, DEVICES, split_axis=0, concat_axis=0, tiled=True)
    values = owned.reshape(local_b, groups // local_b, 2, columns)

    index_b = jnp.arange(local_b, dtype=jnp.int32)
    table_b = block_table(index_b, index_b, local_b, 1.0)
    values = jnp.einsum("pqlm,lhqt->pmht", table_b, values, precision=PRECISE)
    values = values.reshape(2, local_b, size_c * size_d)
    inner = jnp.arange(size_c * size_d, dtype=jnp.int32)
    values = rotate(values, index_b[:, None] * inner[None, :] % column_count, column_count)
    values = values.reshape(2, local_b, size_c, size_d)
    index_c = jnp.arange(size_c, dtype=jnp.int32)
    table_c = block_table(index_c, index_c, size_c, 1.0)
    values = jnp.einsum("pqck,qmcd->pmkd", table_c, values, precision=PRECISE)
    index_d = jnp.arange(size_d, dtype=jnp.int32)
    values = rotate(
        values, (index_c[:, None] * index_d[None, :] % (size_c * size_d))[None], size_c * size_d
    )
    table_d = block_table(index_d, index_d, size_d, 1.0)
    values = jnp.einsum("pqdk,qmcd->pmck", table_d, values, precision=PRECISE)
    return values.reshape(2, 1, 1, local_b, size_c, size_d)


def solution(mesh):
    return jax.shard_map(
        shards,
        mesh=mesh,
        in_specs=(P("wide", "narrow", None, None),),
        out_specs=P(None, "wide", "narrow", None, None, None),
        check_vma=False,
    )
```

```python
import math

import jax
import jax.numpy as jnp
from jax import lax
from jax.sharding import PartitionSpec as P

PRECISE = lax.Precision.HIGHEST
TWO_PI = 2.0 * math.pi
DEVICES = ("wide", "narrow")


def reversed_digits(number, bit_count):
    result = 0 * number
    for position in range(bit_count):
        result = result + number // (1 << position) % 2 * (1 << bit_count - 1 - position)
    return result


def unit_turn(phases, length):
    angles = phases.astype(jnp.float32) * (TWO_PI / length)
    return jnp.cos(angles), jnp.sin(angles)


def block_table(inputs, outputs, length, factor):
    cosine, sines = unit_turn(inputs[:, None] * outputs[None, :] % length, length)
    cosine = cosine * factor
    sines = sines * factor
    return jnp.stack([jnp.stack([cosine, sines]), jnp.stack([-sines, cosine])])


def turn(values, cosine, sines):
    return values[0] * cosine + values[1] * sines, values[1] * cosine - values[0] * sines


def shards(record):
    local_a, local_b, size_c, size_d = record.shape
    wide_size = lax.axis_size("wide")
    narrow_size = lax.axis_size("narrow")
    levels = narrow_size.bit_length() - 1
    size_a = local_a * wide_size
    size_b = local_b * narrow_size
    total_count = size_a * size_b * size_c * size_d
    groups = wide_size * narrow_size
    column_count = local_b * size_c * size_d
    columns = column_count // groups
    here = lax.axis_index(DEVICES)

    gathered = lax.all_to_all(
        record.reshape(groups, columns), DEVICES, split_axis=0, concat_axis=0, tiled=True
    )
    slots = jnp.arange(groups, dtype=jnp.int32)
    frequency = slots // narrow_size + size_a * reversed_digits(slots % narrow_size, levels)
    cosine, sines = unit_turn(frequency[:, None] * slots[None, :] % groups, groups)
    scale = 1.0 / math.sqrt(total_count)
    table = jnp.stack([cosine * scale, -sines * scale], axis=1).reshape(2 * groups, groups)
    column_index = here * columns + jnp.arange(columns, dtype=jnp.int32)
    twiddle = unit_turn(frequency[:, None] * column_index[None, :] % total_count, total_count)
    gathered, table, twiddle = lax.optimization_barrier((gathered, table, twiddle))
    section = jnp.dot(table, gathered, precision=PRECISE).reshape(groups, 2, columns)
    section = jnp.stack(turn((section[:, 0], section[:, 1]), *twiddle), axis=1)
    owned = lax.all_to_all(section, DEVICES, split_axis=0, concat_axis=0, tiled=True)

    index_b = jnp.arange(local_b, dtype=jnp.int32)
    table_b = block_table(index_b, index_b, local_b, 1.0)
    inner = jnp.arange(size_c * size_d, dtype=jnp.int32)
    twiddle_b = unit_turn(index_b[:, None] * inner[None, :] % column_count, column_count)
    index_c = jnp.arange(size_c, dtype=jnp.int32)
    table_c = block_table(index_c, index_c, size_c, 1.0)
    index_d = jnp.arange(size_d, dtype=jnp.int32)
    twiddle_c = unit_turn(index_c[:, None] * index_d[None, :] % (size_c * size_d), size_c * size_d)
    table_d = block_table(index_d, index_d, size_d, 1.0)
    owned, table_b, twiddle_b, table_c, twiddle_c, table_d = lax.optimization_barrier(
        (owned, table_b, twiddle_b, table_c, twiddle_c, table_d)
    )
    values = owned.reshape(local_b, groups // local_b, 2, columns)
    values = jnp.einsum("pqlm,lhqt->pmht", table_b, values, precision=PRECISE)
    values = values.reshape(2, local_b, size_c * size_d)
    values = jnp.stack(turn(values, *twiddle_b)).reshape(2, local_b, size_c, size_d)
    values = jnp.einsum("pqck,qmcd->pmkd", table_c, values, precision=PRECISE)
    values = jnp.stack(turn(values, twiddle_c[0][None], twiddle_c[1][None]))
    values = jnp.einsum("pqdk,qmcd->pmck", table_d, values, precision=PRECISE)
    return values.reshape(2, 1, 1, local_b, size_c, size_d)


def solution(mesh):
    return jax.shard_map(
        shards,
        mesh=mesh,
        in_specs=(P("wide", "narrow", None, None),),
        out_specs=P(None, "wide", "narrow", None, None, None),
        check_vma=False,
    )
```

```python
import math

import jax
import jax.numpy as jnp
from jax import lax
from jax.sharding import PartitionSpec as P

PRECISE = lax.Precision.HIGHEST
TWO_PI = 2.0 * math.pi
DEVICES = ("wide", "narrow")


def reversed_digits(number, bit_count):
    result = 0 * number
    for position in range(bit_count):
        result = result + number // (1 << position) % 2 * (1 << bit_count - 1 - position)
    return result


def unit_turn(phases, length):
    angles = phases.astype(jnp.float32) * (TWO_PI / length)
    return jnp.cos(angles), jnp.sin(angles)


def block_table(inputs, outputs, length, factor):
    cosine, sines = unit_turn(inputs[:, None] * outputs[None, :] % length, length)
    cosine = cosine * factor
    sines = sines * factor
    return jnp.stack([jnp.stack([cosine, sines]), jnp.stack([-sines, cosine])])


def turn(values, cosine, sines):
    return values[0] * cosine + values[1] * sines, values[1] * cosine - values[0] * sines


def shards(record):
    local_a, local_b, size_c, size_d = record.shape
    wide_size = lax.axis_size("wide")
    narrow_size = lax.axis_size("narrow")
    levels = narrow_size.bit_length() - 1
    size_a = local_a * wide_size
    size_b = local_b * narrow_size
    total_count = size_a * size_b * size_c * size_d
    groups = wide_size * narrow_size
    column_count = local_b * size_c * size_d
    columns = column_count // groups
    here = lax.axis_index(DEVICES)

    gathered = lax.all_to_all(
        record.reshape(groups, columns), DEVICES, split_axis=0, concat_axis=0, tiled=True
    )
    slots = jnp.arange(groups, dtype=jnp.int32)
    frequency = slots // narrow_size + size_a * reversed_digits(slots % narrow_size, levels)
    cosine, sines = unit_turn(frequency[:, None] * slots[None, :] % groups, groups)
    scale = 1.0 / math.sqrt(total_count)
    table = jnp.concatenate([cosine * scale, -sines * scale])
    column_index = here * columns + jnp.arange(columns, dtype=jnp.int32)
    twiddle = unit_turn(frequency[:, None] * column_index[None, :] % total_count, total_count)
    gathered, table, twiddle = lax.optimization_barrier((gathered, table, twiddle))
    section = jnp.dot(table, gathered, precision=PRECISE).reshape(2, groups, columns)
    section = jnp.concatenate(turn(section, *twiddle), axis=1)
    owned = lax.all_to_all(section, DEVICES, split_axis=0, concat_axis=0, tiled=True)

    index_b = jnp.arange(local_b, dtype=jnp.int32)
    table_b = block_table(index_b, index_b, local_b, 1.0)
    inner = jnp.arange(size_c * size_d, dtype=jnp.int32)
    twiddle_b = unit_turn(index_b[:, None] * inner[None, :] % column_count, column_count)
    index_c = jnp.arange(size_c, dtype=jnp.int32)
    table_c = block_table(index_c, index_c, size_c, 1.0)
    index_d = jnp.arange(size_d, dtype=jnp.int32)
    twiddle_c = unit_turn(index_c[:, None] * index_d[None, :] % (size_c * size_d), size_c * size_d)
    table_d = block_table(index_d, index_d, size_d, 1.0)
    owned, table_b, twiddle_b, table_c, twiddle_c, table_d = lax.optimization_barrier(
        (owned, table_b, twiddle_b, table_c, twiddle_c, table_d)
    )
    values = owned.reshape(local_b, groups // local_b, 2, columns)
    values = jnp.einsum("pqlm,lhqt->pmht", table_b, values, precision=PRECISE)
    values = values.reshape(2, local_b, size_c * size_d)
    values = jnp.stack(turn(values, *twiddle_b)).reshape(2, local_b, size_c, size_d)
    values = jnp.einsum("pqck,qmcd->pmkd", table_c, values, precision=PRECISE)
    values = jnp.stack(turn(values, twiddle_c[0][None], twiddle_c[1][None]))
    values = jnp.einsum("pqdk,qmcd->pmck", table_d, values, precision=PRECISE)
    return values.reshape(2, 1, 1, local_b, size_c, size_d)


def solution(mesh):
    return jax.shard_map(
        shards,
        mesh=mesh,
        in_specs=(P("wide", "narrow", None, None),),
        out_specs=P(None, "wide", "narrow", None, None, None),
        check_vma=False,
    )
```

```python
import math

import jax
import jax.numpy as jnp
from jax import lax
from jax.sharding import PartitionSpec as P

PRECISE = lax.Precision.HIGH
TWO_PI = 2.0 * math.pi
DEVICES = ("wide", "narrow")


def reversed_digits(number, bit_count):
    result = 0 * number
    for position in range(bit_count):
        result = result + number // (1 << position) % 2 * (1 << bit_count - 1 - position)
    return result


def unit_turn(phases, length):
    angles = phases.astype(jnp.float32) * (TWO_PI / length)
    return jnp.cos(angles), jnp.sin(angles)


def block_table(inputs, outputs, length, factor):
    cosine, sines = unit_turn(inputs[:, None] * outputs[None, :] % length, length)
    cosine = cosine * factor
    sines = sines * factor
    return jnp.stack([jnp.stack([cosine, sines]), jnp.stack([-sines, cosine])])


def turn(values, cosine, sines):
    return values[0] * cosine + values[1] * sines, values[1] * cosine - values[0] * sines


def shards(record):
    local_a, local_b, size_c, size_d = record.shape
    wide_size = lax.axis_size("wide")
    narrow_size = lax.axis_size("narrow")
    levels = narrow_size.bit_length() - 1
    size_a = local_a * wide_size
    size_b = local_b * narrow_size
    total_count = size_a * size_b * size_c * size_d
    groups = wide_size * narrow_size
    column_count = local_b * size_c * size_d
    columns = column_count // groups
    here = lax.axis_index(DEVICES)

    gathered = lax.all_to_all(
        record.reshape(groups, columns), DEVICES, split_axis=0, concat_axis=0, tiled=True
    )
    slots = jnp.arange(groups, dtype=jnp.int32)
    frequency = slots // narrow_size + size_a * reversed_digits(slots % narrow_size, levels)
    cosine, sines = unit_turn(frequency[:, None] * slots[None, :] % groups, groups)
    scale = 1.0 / math.sqrt(total_count)
    table = jnp.concatenate([cosine * scale, -sines * scale])
    column_index = here * columns + jnp.arange(columns, dtype=jnp.int32)
    twiddle = unit_turn(frequency[:, None] * column_index[None, :] % total_count, total_count)
    gathered, table, twiddle = lax.optimization_barrier((gathered, table, twiddle))
    section = jnp.dot(table, gathered, precision=PRECISE).reshape(2, groups, columns)
    section = jnp.concatenate(turn(section, *twiddle), axis=1)
    owned = lax.all_to_all(section, DEVICES, split_axis=0, concat_axis=0, tiled=True)

    index_b = jnp.arange(local_b, dtype=jnp.int32)
    table_b = block_table(index_b, index_b, local_b, 1.0)
    inner = jnp.arange(size_c * size_d, dtype=jnp.int32)
    twiddle_b = unit_turn(index_b[:, None] * inner[None, :] % column_count, column_count)
    index_c = jnp.arange(size_c, dtype=jnp.int32)
    table_c = block_table(index_c, index_c, size_c, 1.0)
    index_d = jnp.arange(size_d, dtype=jnp.int32)
    twiddle_c = unit_turn(index_c[:, None] * index_d[None, :] % (size_c * size_d), size_c * size_d)
    table_d = block_table(index_d, index_d, size_d, 1.0)
    owned, table_b, twiddle_b, table_c, twiddle_c, table_d = lax.optimization_barrier(
        (owned, table_b, twiddle_b, table_c, twiddle_c, table_d)
    )
    values = owned.reshape(local_b, groups // local_b, 2, columns)
    values = jnp.einsum("pqlm,lhqt->pmht", table_b, values, precision=PRECISE)
    values = values.reshape(2, local_b, size_c * size_d)
    values = jnp.stack(turn(values, *twiddle_b)).reshape(2, local_b, size_c, size_d)
    values = jnp.einsum("pqck,qmcd->pmkd", table_c, values, precision=PRECISE)
    values = jnp.stack(turn(values, twiddle_c[0][None], twiddle_c[1][None]))
    values = jnp.einsum("pqdk,qmcd->pmck", table_d, values, precision=PRECISE)
    return values.reshape(2, 1, 1, local_b, size_c, size_d)


def solution(mesh):
    return jax.shard_map(
        shards,
        mesh=mesh,
        in_specs=(P("wide", "narrow", None, None),),
        out_specs=P(None, "wide", "narrow", None, None, None),
        check_vma=False,
    )
```

```python
import math

import jax
import jax.numpy as jnp
from jax import lax
from jax.experimental.layout import Layout, with_layout_constraint
from jax.sharding import PartitionSpec as P

PRECISE = lax.Precision.HIGH
TWO_PI = 2.0 * math.pi
DEVICES = ("wide", "narrow")
LANES = 128


def reversed_digits(number, bit_count):
    result = 0 * number
    for position in range(bit_count):
        result = result + number // (1 << position) % 2 * (1 << bit_count - 1 - position)
    return result


def unit_turn(phases, length):
    angles = phases.astype(jnp.float32) * (TWO_PI / length)
    return jnp.cos(angles), jnp.sin(angles)


def block_table(inputs, outputs, length, factor):
    cosine, sines = unit_turn(inputs[:, None] * outputs[None, :] % length, length)
    cosine = cosine * factor
    sines = sines * factor
    return jnp.stack([jnp.stack([cosine, sines]), jnp.stack([-sines, cosine])])


def turn(values, cosine, sines):
    return values[0] * cosine + values[1] * sines, values[1] * cosine - values[0] * sines


def shards(record):
    local_a, local_b, size_c, size_d = record.shape
    wide_size = lax.axis_size("wide")
    narrow_size = lax.axis_size("narrow")
    levels = narrow_size.bit_length() - 1
    size_a = local_a * wide_size
    size_b = local_b * narrow_size
    total_count = size_a * size_b * size_c * size_d
    groups = wide_size * narrow_size
    column_count = local_b * size_c * size_d
    columns = column_count // groups
    here = lax.axis_index(DEVICES)

    gathered = lax.all_to_all(
        record.reshape(groups, columns), DEVICES, split_axis=0, concat_axis=0, tiled=True
    )
    slots = jnp.arange(groups, dtype=jnp.int32)
    frequency = slots // narrow_size + size_a * reversed_digits(slots % narrow_size, levels)
    cosine, sines = unit_turn(frequency[:, None] * slots[None, :] % groups, groups)
    scale = 1.0 / math.sqrt(total_count)
    table = jnp.concatenate([cosine * scale, -sines * scale])
    column_index = here * columns + jnp.arange(columns, dtype=jnp.int32)
    twiddle = unit_turn(frequency[:, None] * column_index[None, :] % total_count, total_count)
    gathered, table, twiddle = lax.optimization_barrier((gathered, table, twiddle))
    section = with_layout_constraint(
        jnp.dot(table, gathered, precision=PRECISE), Layout(major_to_minor=(0, 1))
    ).reshape(2, groups, columns)
    section = jnp.concatenate(turn(section, *twiddle), axis=1).reshape(groups, -1, LANES)
    owned = lax.all_to_all(section, DEVICES, split_axis=0, concat_axis=0, tiled=True)

    index_b = jnp.arange(local_b, dtype=jnp.int32)
    table_b = block_table(index_b, index_b, local_b, 1.0)
    inner = jnp.arange(size_c * size_d, dtype=jnp.int32)
    twiddle_b = unit_turn(index_b[:, None] * inner[None, :] % column_count, column_count)
    index_c = jnp.arange(size_c, dtype=jnp.int32)
    table_c = block_table(index_c, index_c, size_c, 1.0)
    index_d = jnp.arange(size_d, dtype=jnp.int32)
    twiddle_c = unit_turn(index_c[:, None] * index_d[None, :] % (size_c * size_d), size_c * size_d)
    table_d = block_table(index_d, index_d, size_d, 1.0)
    owned, table_b, twiddle_b, table_c, twiddle_c, table_d = lax.optimization_barrier(
        (owned, table_b, twiddle_b, table_c, twiddle_c, table_d)
    )
    rows = owned.shape[1] // 2
    values = owned.reshape(local_b, groups // local_b, 2 * rows, LANES)
    halves = with_layout_constraint(
        jnp.einsum("pml,lhrc->pmhrc", table_b[0], values, precision=PRECISE),
        Layout(major_to_minor=(0, 1, 2, 3, 4)),
    )
    values = jnp.stack(
        [
            halves[0, :, :, :rows] + halves[1, :, :, rows:],
            halves[0, :, :, rows:] - halves[1, :, :, :rows],
        ]
    ).reshape(2, local_b, size_c * size_d)
    values = jnp.stack(turn(values, *twiddle_b)).reshape(2, local_b, size_c, size_d)
    values = jnp.einsum("pqck,qmcd->pmkd", table_c, values, precision=PRECISE)
    values = jnp.stack(turn(values, twiddle_c[0][None], twiddle_c[1][None]))
    values = jnp.einsum("pqdk,qmcd->pmck", table_d, values, precision=PRECISE)
    return values.reshape(2, 1, 1, local_b, size_c, size_d)


def solution(mesh):
    return jax.shard_map(
        shards,
        mesh=mesh,
        in_specs=(P("wide", "narrow", None, None),),
        out_specs=P(None, "wide", "narrow", None, None, None),
        check_vma=False,
    )
```

```python
import math

import jax
import jax.numpy as jnp
from jax import lax
from jax.experimental.layout import Layout, with_layout_constraint
from jax.sharding import PartitionSpec as P

PRECISE = lax.Precision.HIGH
TWO_PI = 2.0 * math.pi
DEVICES = ("wide", "narrow")
LANES = 128


def reversed_digits(number, bit_count):
    result = 0 * number
    for position in range(bit_count):
        result = result + number // (1 << position) % 2 * (1 << bit_count - 1 - position)
    return result


def unit_turn(phases, length):
    angles = phases.astype(jnp.float32) * (TWO_PI / length)
    return jnp.cos(angles), jnp.sin(angles)


def block_table(inputs, outputs, length, factor):
    cosine, sines = unit_turn(inputs[:, None] * outputs[None, :] % length, length)
    cosine = cosine * factor
    sines = sines * factor
    return jnp.stack([jnp.stack([cosine, sines]), jnp.stack([-sines, cosine])])


def turn(values, cosine, sines):
    return values[0] * cosine + values[1] * sines, values[1] * cosine - values[0] * sines


def shards(record):
    local_a, local_b, size_c, size_d = record.shape
    wide_size = lax.axis_size("wide")
    narrow_size = lax.axis_size("narrow")
    levels = narrow_size.bit_length() - 1
    size_a = local_a * wide_size
    size_b = local_b * narrow_size
    total_count = size_a * size_b * size_c * size_d
    groups = wide_size * narrow_size
    column_count = local_b * size_c * size_d
    columns = column_count // groups
    here = lax.axis_index(DEVICES)

    gathered = lax.all_to_all(
        record.reshape(groups, columns), DEVICES, split_axis=0, concat_axis=0, tiled=True
    )
    slots = jnp.arange(groups, dtype=jnp.int32)
    frequency = slots // narrow_size + size_a * reversed_digits(slots % narrow_size, levels)
    cosine, sines = unit_turn(frequency[:, None] * slots[None, :] % groups, groups)
    scale = 1.0 / math.sqrt(total_count)
    table = jnp.concatenate([cosine * scale, -sines * scale])
    column_index = here * columns + jnp.arange(columns, dtype=jnp.int32)
    twiddle = unit_turn(frequency[:, None] * column_index[None, :] % total_count, total_count)
    gathered, table, twiddle = lax.optimization_barrier((gathered, table, twiddle))
    section = with_layout_constraint(
        jnp.dot(table, gathered, precision=PRECISE), Layout(major_to_minor=(0, 1))
    ).reshape(2, groups, columns)
    section = jnp.concatenate(turn(section, *twiddle), axis=1).reshape(groups, -1, LANES)
    owned = lax.all_to_all(section, DEVICES, split_axis=0, concat_axis=0, tiled=True)

    index_b = jnp.arange(local_b, dtype=jnp.int32)
    table_b = block_table(index_b, index_b, local_b, 1.0)
    inner = jnp.arange(size_c * size_d, dtype=jnp.int32)
    twiddle_b = unit_turn(index_b[:, None] * inner[None, :] % column_count, column_count)
    index_c = jnp.arange(size_c, dtype=jnp.int32)
    table_c = block_table(index_c, index_c, size_c, 1.0)
    index_d = jnp.arange(size_d, dtype=jnp.int32)
    twiddle_c = unit_turn(index_c[:, None] * index_d[None, :] % (size_c * size_d), size_c * size_d)
    table_d = block_table(index_d, index_d, size_d, 1.0)
    owned, table_b, twiddle_b, table_c, twiddle_c, table_d = lax.optimization_barrier(
        (owned, table_b, twiddle_b, table_c, twiddle_c, table_d)
    )
    values = owned.reshape(local_b, groups // local_b, 2, columns)
    values = jnp.einsum("pqlm,lhqt->pmht", table_b, values, precision=PRECISE)
    values = values.reshape(2, local_b, size_c * size_d)
    values = jnp.stack(turn(values, *twiddle_b)).reshape(2, local_b, size_c, size_d)
    values = jnp.einsum("pqck,qmcd->pmkd", table_c, values, precision=PRECISE)
    values = jnp.stack(turn(values, twiddle_c[0][None], twiddle_c[1][None]))
    values = jnp.einsum("pqdk,qmcd->pmck", table_d, values, precision=PRECISE)
    return values.reshape(2, 1, 1, local_b, size_c, size_d)


def solution(mesh):
    return jax.shard_map(
        shards,
        mesh=mesh,
        in_specs=(P("wide", "narrow", None, None),),
        out_specs=P(None, "wide", "narrow", None, None, None),
        check_vma=False,
    )
```

```python
import math

import jax
import jax.numpy as jnp
from jax import lax
from jax.experimental.layout import Layout, with_layout_constraint
from jax.sharding import PartitionSpec as P

PRECISE = lax.Precision.HIGH
TWO_PI = 2.0 * math.pi
DEVICES = ("wide", "narrow")
LANES = 128


def reversed_digits(number, bit_count):
    result = 0 * number
    for position in range(bit_count):
        result = result + number // (1 << position) % 2 * (1 << bit_count - 1 - position)
    return result


def unit_turn(phases, length):
    angles = phases.astype(jnp.float32) * (TWO_PI / length)
    return jnp.cos(angles), jnp.sin(angles)


def block_table(inputs, outputs, length, factor):
    cosine, sines = unit_turn(inputs[:, None] * outputs[None, :] % length, length)
    cosine = cosine * factor
    sines = sines * factor
    return jnp.stack([jnp.stack([cosine, sines]), jnp.stack([-sines, cosine])])


def turn(values, cosine, sines):
    return values[0] * cosine + values[1] * sines, values[1] * cosine - values[0] * sines


def shards(record):
    local_a, local_b, size_c, size_d = record.shape
    wide_size = lax.axis_size("wide")
    narrow_size = lax.axis_size("narrow")
    levels = narrow_size.bit_length() - 1
    size_a = local_a * wide_size
    size_b = local_b * narrow_size
    total_count = size_a * size_b * size_c * size_d
    groups = wide_size * narrow_size
    column_count = local_b * size_c * size_d
    columns = column_count // groups
    here = lax.axis_index(DEVICES)

    gathered = lax.all_to_all(
        record.reshape(groups, columns), DEVICES, split_axis=0, concat_axis=0, tiled=True
    )
    slots = jnp.arange(groups, dtype=jnp.int32)
    frequency = slots // narrow_size + size_a * reversed_digits(slots % narrow_size, levels)
    cosine, sines = unit_turn(frequency[:, None] * slots[None, :] % groups, groups)
    scale = 1.0 / math.sqrt(total_count)
    table = jnp.concatenate([cosine * scale, -sines * scale])
    column_index = here * columns + jnp.arange(columns, dtype=jnp.int32)
    twiddle = unit_turn(frequency[:, None] * column_index[None, :] % total_count, total_count)
    gathered, table, twiddle = lax.optimization_barrier((gathered, table, twiddle))
    section = with_layout_constraint(
        jnp.dot(table, gathered, precision=PRECISE), Layout(major_to_minor=(0, 1))
    ).reshape(2, groups, columns)
    section = jnp.concatenate(turn(section, *twiddle), axis=1).reshape(groups, -1, LANES)
    owned = lax.all_to_all(section, DEVICES, split_axis=0, concat_axis=0, tiled=True)

    index_b = jnp.arange(local_b, dtype=jnp.int32)
    table_b = block_table(index_b, index_b, local_b, 1.0)
    inner = jnp.arange(size_c * size_d, dtype=jnp.int32)
    twiddle_b = unit_turn(index_b[:, None] * inner[None, :] % column_count, column_count)
    index_c = jnp.arange(size_c, dtype=jnp.int32)
    table_c = block_table(index_c, index_c, size_c, 1.0)
    index_d = jnp.arange(size_d, dtype=jnp.int32)
    twiddle_c = unit_turn(index_c[:, None] * index_d[None, :] % (size_c * size_d), size_c * size_d)
    table_d = block_table(index_d, index_d, size_d, 1.0)
    owned, table_b, twiddle_b, table_c, twiddle_c, table_d = lax.optimization_barrier(
        (owned, table_b, twiddle_b, table_c, twiddle_c, table_d)
    )
    values = owned.reshape(local_b, groups // local_b, 2, columns)
    values = jnp.einsum("pqlm,lhqt->pmht", table_b, values, precision=PRECISE)
    values = values.reshape(2, local_b, size_c * size_d)
    values = jnp.stack(turn(values, *twiddle_b)).reshape(2, local_b, size_c, size_d)
    values = jnp.einsum("pqck,qmcd->pmkd", table_c, values, precision=PRECISE)
    values = jnp.stack(turn(values, twiddle_c[0][None], twiddle_c[1][None]))
    values = jnp.broadcast_to(values.reshape(1, 2, local_b * size_c, size_d), (2,) + values.shape[:1] + (local_b * size_c, size_d))
    values = jnp.einsum("pqdk,pqnd->pnk", table_d, values, precision=PRECISE)
    return values.reshape(2, 1, 1, local_b, size_c, size_d)


def solution(mesh):
    return jax.shard_map(
        shards,
        mesh=mesh,
        in_specs=(P("wide", "narrow", None, None),),
        out_specs=P(None, "wide", "narrow", None, None, None),
        check_vma=False,
    )
```

```python
import math

import jax
import jax.numpy as jnp
from jax import lax
from jax.experimental.layout import Layout, with_layout_constraint
from jax.sharding import PartitionSpec as P

PRECISE = lax.Precision.HIGH
TWO_PI = 2.0 * math.pi
DEVICES = ("wide", "narrow")
LANES = 128


def reversed_digits(number, bit_count):
    result = 0 * number
    for position in range(bit_count):
        result = result + number // (1 << position) % 2 * (1 << bit_count - 1 - position)
    return result


def unit_turn(phases, length):
    angles = phases.astype(jnp.float32) * (TWO_PI / length)
    return jnp.cos(angles), jnp.sin(angles)


def block_table(inputs, outputs, length, factor):
    cosine, sines = unit_turn(inputs[:, None] * outputs[None, :] % length, length)
    cosine = cosine * factor
    sines = sines * factor
    return jnp.stack([jnp.stack([cosine, sines]), jnp.stack([-sines, cosine])])


def turn(values, cosine, sines):
    return values[0] * cosine + values[1] * sines, values[1] * cosine - values[0] * sines


def shards(record):
    local_a, local_b, size_c, size_d = record.shape
    wide_size = lax.axis_size("wide")
    narrow_size = lax.axis_size("narrow")
    levels = narrow_size.bit_length() - 1
    size_a = local_a * wide_size
    size_b = local_b * narrow_size
    total_count = size_a * size_b * size_c * size_d
    groups = wide_size * narrow_size
    column_count = local_b * size_c * size_d
    columns = column_count // groups
    here = lax.axis_index(DEVICES)

    gathered = lax.all_to_all(
        record.reshape(groups, columns), DEVICES, split_axis=0, concat_axis=0, tiled=True
    )
    slots = jnp.arange(groups, dtype=jnp.int32)
    frequency = slots // narrow_size + size_a * reversed_digits(slots % narrow_size, levels)
    cosine, sines = unit_turn(frequency[:, None] * slots[None, :] % groups, groups)
    scale = 1.0 / math.sqrt(total_count)
    table = jnp.concatenate([cosine * scale, -sines * scale])
    column_index = here * columns + jnp.arange(columns, dtype=jnp.int32)
    twiddle = unit_turn(frequency[:, None] * column_index[None, :] % total_count, total_count)
    gathered, table, twiddle = lax.optimization_barrier((gathered, table, twiddle))
    section = with_layout_constraint(
        jnp.dot(table, gathered, precision=PRECISE), Layout(major_to_minor=(0, 1))
    ).reshape(2, groups, columns)
    section = with_layout_constraint(
        jnp.stack(turn(section, *twiddle), axis=1), Layout((0, 1, 2))
    )
    owned = lax.all_to_all(section, DEVICES, split_axis=0, concat_axis=0, tiled=True)

    index_b = jnp.arange(local_b, dtype=jnp.int32)
    table_b = block_table(index_b, index_b, local_b, 1.0)
    inner = jnp.arange(size_c * size_d, dtype=jnp.int32)
    twiddle_b = unit_turn(index_b[:, None] * inner[None, :] % column_count, column_count)
    index_c = jnp.arange(size_c, dtype=jnp.int32)
    table_c = block_table(index_c, index_c, size_c, 1.0)
    index_d = jnp.arange(size_d, dtype=jnp.int32)
    twiddle_c = unit_turn(index_c[:, None] * index_d[None, :] % (size_c * size_d), size_c * size_d)
    table_d = block_table(index_d, index_d, size_d, 1.0)
    owned, table_b, twiddle_b, table_c, twiddle_c, table_d = lax.optimization_barrier(
        (owned, table_b, twiddle_b, table_c, twiddle_c, table_d)
    )
    values = owned.reshape(local_b, groups // local_b, 2, columns)
    values = jnp.einsum("pqlm,lhqt->pmht", table_b, values, precision=PRECISE)
    values = values.reshape(2, local_b, size_c * size_d)
    values = jnp.stack(turn(values, *twiddle_b)).reshape(2, local_b, size_c, size_d)
    values = jnp.einsum("pqck,qmcd->pmkd", table_c, values, precision=PRECISE)
    values = jnp.stack(turn(values, twiddle_c[0][None], twiddle_c[1][None]))
    values = jnp.einsum("pqdk,qmcd->pmck", table_d, values, precision=PRECISE)
    return values.reshape(2, 1, 1, local_b, size_c, size_d)


def solution(mesh):
    return jax.shard_map(
        shards,
        mesh=mesh,
        in_specs=(P("wide", "narrow", None, None),),
        out_specs=P(None, "wide", "narrow", None, None, None),
        check_vma=False,
    )
```

```python
import math

import jax
import jax.numpy as jnp
from jax import lax
from jax.experimental.layout import Layout, with_layout_constraint
from jax.sharding import PartitionSpec as P

PRECISE = lax.Precision.HIGH
TWO_PI = 2.0 * math.pi
DEVICES = ("wide", "narrow")
LANES = 128


def reversed_digits(number, bit_count):
    result = 0 * number
    for position in range(bit_count):
        result = result + number // (1 << position) % 2 * (1 << bit_count - 1 - position)
    return result


def unit_turn(phases, length):
    angles = phases.astype(jnp.float32) * (TWO_PI / length)
    return jnp.cos(angles), jnp.sin(angles)


def block_table(inputs, outputs, length, factor):
    cosine, sines = unit_turn(inputs[:, None] * outputs[None, :] % length, length)
    cosine = cosine * factor
    sines = sines * factor
    return jnp.stack([jnp.stack([cosine, sines]), jnp.stack([-sines, cosine])])


def turn(values, cosine, sines):
    return values[0] * cosine + values[1] * sines, values[1] * cosine - values[0] * sines


def shards(record):
    local_a, local_b, size_c, size_d = record.shape
    wide_size = lax.axis_size("wide")
    narrow_size = lax.axis_size("narrow")
    levels = narrow_size.bit_length() - 1
    size_a = local_a * wide_size
    size_b = local_b * narrow_size
    total_count = size_a * size_b * size_c * size_d
    groups = wide_size * narrow_size
    column_count = local_b * size_c * size_d
    columns = column_count // groups
    here = lax.axis_index(DEVICES)

    gathered = lax.all_to_all(
        record.reshape(groups, columns), DEVICES, split_axis=0, concat_axis=0, tiled=True
    )
    slots = jnp.arange(groups, dtype=jnp.int32)
    frequency = slots // narrow_size + size_a * reversed_digits(slots % narrow_size, levels)
    cosine, sines = unit_turn(frequency[:, None] * slots[None, :] % groups, groups)
    scale = 1.0 / math.sqrt(total_count)
    table = jnp.concatenate([cosine * scale, -sines * scale])
    column_index = here * columns + jnp.arange(columns, dtype=jnp.int32)
    twiddle = unit_turn(frequency[:, None] * column_index[None, :] % total_count, total_count)
    gathered, table, twiddle = lax.optimization_barrier((gathered, table, twiddle))
    section = with_layout_constraint(
        jnp.dot(table, gathered, precision=PRECISE), Layout(major_to_minor=(0, 1))
    ).reshape(2, groups, columns)
    real, imag = (part[:, None] for part in turn(section, *twiddle))
    part_index = lax.broadcasted_iota(jnp.int32, (groups, 2, columns), 1)
    section = with_layout_constraint(jnp.where(part_index == 0, real, imag), Layout((0, 1, 2)))
    owned = lax.all_to_all(section, DEVICES, split_axis=0, concat_axis=0, tiled=True)

    index_b = jnp.arange(local_b, dtype=jnp.int32)
    table_b = block_table(index_b, index_b, local_b, 1.0)
    inner = jnp.arange(size_c * size_d, dtype=jnp.int32)
    twiddle_b = unit_turn(index_b[:, None] * inner[None, :] % column_count, column_count)
    index_c = jnp.arange(size_c, dtype=jnp.int32)
    table_c = block_table(index_c, index_c, size_c, 1.0)
    index_d = jnp.arange(size_d, dtype=jnp.int32)
    twiddle_c = unit_turn(index_c[:, None] * index_d[None, :] % (size_c * size_d), size_c * size_d)
    table_d = block_table(index_d, index_d, size_d, 1.0)
    owned, table_b, twiddle_b, table_c, twiddle_c, table_d = lax.optimization_barrier(
        (owned, table_b, twiddle_b, table_c, twiddle_c, table_d)
    )
    values = owned.reshape(local_b, groups // local_b, 2, columns)
    values = jnp.einsum("pqlm,lhqt->pmht", table_b, values, precision=PRECISE)
    values = values.reshape(2, local_b, size_c * size_d)
    values = jnp.stack(turn(values, *twiddle_b)).reshape(2, local_b, size_c, size_d)
    values = jnp.einsum("pqck,qmcd->pmkd", table_c, values, precision=PRECISE)
    values = jnp.stack(turn(values, twiddle_c[0][None], twiddle_c[1][None]))
    values = jnp.einsum("pqdk,qmcd->pmck", table_d, values, precision=PRECISE)
    return values.reshape(2, 1, 1, local_b, size_c, size_d)


def solution(mesh):
    return jax.shard_map(
        shards,
        mesh=mesh,
        in_specs=(P("wide", "narrow", None, None),),
        out_specs=P(None, "wide", "narrow", None, None, None),
        check_vma=False,
    )
```

```python
import math

import jax
import jax.numpy as jnp
from jax import lax
from jax.experimental.layout import Layout, with_layout_constraint
from jax.sharding import PartitionSpec as P

PRECISE = lax.Precision.HIGH
TWO_PI = 2.0 * math.pi
DEVICES = ("wide", "narrow")
LANES = 128


def reversed_digits(number, bit_count):
    result = 0 * number
    for position in range(bit_count):
        result = result + number // (1 << position) % 2 * (1 << bit_count - 1 - position)
    return result


def unit_turn(phases, length):
    angles = phases.astype(jnp.float32) * (TWO_PI / length)
    return jnp.cos(angles), jnp.sin(angles)


def block_table(inputs, outputs, length, factor):
    cosine, sines = unit_turn(inputs[:, None] * outputs[None, :] % length, length)
    cosine = cosine * factor
    sines = sines * factor
    return jnp.stack([jnp.stack([cosine, sines]), jnp.stack([-sines, cosine])])


def turn(values, cosine, sines):
    return values[0] * cosine + values[1] * sines, values[1] * cosine - values[0] * sines


def shards(record):
    local_a, local_b, size_c, size_d = record.shape
    wide_size = lax.axis_size("wide")
    narrow_size = lax.axis_size("narrow")
    levels = narrow_size.bit_length() - 1
    size_a = local_a * wide_size
    size_b = local_b * narrow_size
    total_count = size_a * size_b * size_c * size_d
    groups = wide_size * narrow_size
    column_count = local_b * size_c * size_d
    columns = column_count // groups
    here = lax.axis_index(DEVICES)

    gathered = lax.all_to_all(
        record.reshape(groups, columns), DEVICES, split_axis=0, concat_axis=0, tiled=True
    )
    slots = jnp.arange(groups, dtype=jnp.int32)
    frequency = slots // narrow_size + size_a * reversed_digits(slots % narrow_size, levels)
    cosine, sines = unit_turn(frequency[:, None] * slots[None, :] % groups, groups)
    scale = 1.0 / math.sqrt(total_count)
    table = jnp.concatenate([cosine * scale, -sines * scale])
    column_index = here * columns + jnp.arange(columns, dtype=jnp.int32)
    twiddle = unit_turn(frequency[:, None] * column_index[None, :] % total_count, total_count)
    gathered, table, twiddle = lax.optimization_barrier((gathered, table, twiddle))
    section = with_layout_constraint(
        jnp.dot(table, gathered, precision=PRECISE), Layout(major_to_minor=(0, 1))
    ).reshape(2, groups, columns)
    first = lax.broadcasted_iota(jnp.int32, (groups, 2, columns), 1) == 0
    real, imag = section[0][:, None], section[1][:, None]
    cosine, sines = twiddle[0][:, None], twiddle[1][:, None]
    section = jnp.where(first, real, imag) * cosine + jnp.where(first, imag, -real) * sines
    section = with_layout_constraint(section, Layout((0, 1, 2)))
    owned = lax.all_to_all(section, DEVICES, split_axis=0, concat_axis=0, tiled=True)

    index_b = jnp.arange(local_b, dtype=jnp.int32)
    table_b = block_table(index_b, index_b, local_b, 1.0)
    inner = jnp.arange(size_c * size_d, dtype=jnp.int32)
    twiddle_b = unit_turn(index_b[:, None] * inner[None, :] % column_count, column_count)
    index_c = jnp.arange(size_c, dtype=jnp.int32)
    table_c = block_table(index_c, index_c, size_c, 1.0)
    index_d = jnp.arange(size_d, dtype=jnp.int32)
    twiddle_c = unit_turn(index_c[:, None] * index_d[None, :] % (size_c * size_d), size_c * size_d)
    table_d = block_table(index_d, index_d, size_d, 1.0)
    owned, table_b, twiddle_b, table_c, twiddle_c, table_d = lax.optimization_barrier(
        (owned, table_b, twiddle_b, table_c, twiddle_c, table_d)
    )
    values = owned.reshape(local_b, groups // local_b, 2, columns)
    values = jnp.einsum("pqlm,lhqt->pmht", table_b, values, precision=PRECISE)
    values = values.reshape(2, local_b, size_c * size_d)
    values = jnp.stack(turn(values, *twiddle_b)).reshape(2, local_b, size_c, size_d)
    values = jnp.einsum("pqck,qmcd->pmkd", table_c, values, precision=PRECISE)
    values = jnp.stack(turn(values, twiddle_c[0][None], twiddle_c[1][None]))
    values = jnp.einsum("pqdk,qmcd->pmck", table_d, values, precision=PRECISE)
    return values.reshape(2, 1, 1, local_b, size_c, size_d)


def solution(mesh):
    return jax.shard_map(
        shards,
        mesh=mesh,
        in_specs=(P("wide", "narrow", None, None),),
        out_specs=P(None, "wide", "narrow", None, None, None),
        check_vma=False,
    )
```

```python
import math

import jax
import jax.numpy as jnp
from jax import lax
from jax.experimental.layout import Layout, with_layout_constraint
from jax.sharding import PartitionSpec as P

PRECISE = lax.Precision.HIGH
TWO_PI = 2.0 * math.pi
DEVICES = ("wide", "narrow")
LANES = 128


def reversed_digits(number, bit_count):
    result = 0 * number
    for position in range(bit_count):
        result = result + number // (1 << position) % 2 * (1 << bit_count - 1 - position)
    return result


def unit_turn(phases, length):
    angles = phases.astype(jnp.float32) * (TWO_PI / length)
    return jnp.cos(angles), jnp.sin(angles)


def block_table(inputs, outputs, length, factor):
    cosine, sines = unit_turn(inputs[:, None] * outputs[None, :] % length, length)
    cosine = cosine * factor
    sines = sines * factor
    return jnp.stack([jnp.stack([cosine, sines]), jnp.stack([-sines, cosine])])


def turn(values, cosine, sines):
    return values[0] * cosine + values[1] * sines, values[1] * cosine - values[0] * sines


def shards(record):
    local_a, local_b, size_c, size_d = record.shape
    wide_size = lax.axis_size("wide")
    narrow_size = lax.axis_size("narrow")
    levels = narrow_size.bit_length() - 1
    size_a = local_a * wide_size
    size_b = local_b * narrow_size
    total_count = size_a * size_b * size_c * size_d
    groups = wide_size * narrow_size
    column_count = local_b * size_c * size_d
    columns = column_count // groups
    here = lax.axis_index(DEVICES)

    gathered = lax.all_to_all(
        record.reshape(groups, columns), DEVICES, split_axis=0, concat_axis=0, tiled=True
    )
    slots = jnp.arange(groups, dtype=jnp.int32)
    frequency = slots // narrow_size + size_a * reversed_digits(slots % narrow_size, levels)
    cosine, sines = unit_turn(frequency[:, None] * slots[None, :] % groups, groups)
    scale = 1.0 / math.sqrt(total_count)
    table = jnp.concatenate([cosine * scale, -sines * scale])
    column_index = here * columns + jnp.arange(columns, dtype=jnp.int32)
    twiddle = unit_turn(frequency[:, None] * column_index[None, :] % total_count, total_count)
    gathered, table, twiddle = lax.optimization_barrier((gathered, table, twiddle))
    section = with_layout_constraint(
        jnp.dot(table, gathered, precision=PRECISE), Layout(major_to_minor=(0, 1))
    ).reshape(2, groups, columns)
    real, imag = (part[:, None] for part in turn(section, *twiddle))
    part_index = lax.broadcasted_iota(jnp.int32, (groups, 2, columns), 1)
    section = with_layout_constraint(jnp.where(part_index == 0, real, imag), Layout((0, 1, 2)))
    owned = lax.all_to_all(section, DEVICES, split_axis=0, concat_axis=0, tiled=True)

    index_b = jnp.arange(local_b, dtype=jnp.int32)
    table_b = block_table(index_b, index_b, local_b, 1.0)
    inner = jnp.arange(size_c * size_d, dtype=jnp.int32)
    twiddle_b = unit_turn(index_b[:, None] * inner[None, :] % column_count, column_count)
    index_c = jnp.arange(size_c, dtype=jnp.int32)
    table_c = block_table(index_c, index_c, size_c, 1.0)
    index_d = jnp.arange(size_d, dtype=jnp.int32)
    twiddle_c = unit_turn(index_c[:, None] * index_d[None, :] % (size_c * size_d), size_c * size_d)
    table_d = block_table(index_d, index_d, size_d, 1.0)
    owned, table_b, twiddle_b, table_c, twiddle_c, table_d = lax.optimization_barrier(
        (owned, table_b, twiddle_b, table_c, twiddle_c, table_d)
    )
    values = owned.reshape(local_b, groups // local_b, 2, columns)
    values = jnp.einsum("pqlm,lhqt->pmht", table_b, values, precision=PRECISE)
    values = values.reshape(2, local_b, size_c * size_d)
    values = jnp.stack(turn(values, *twiddle_b)).reshape(2, local_b, size_c, size_d)
    values = jnp.einsum("pqck,qmcd->pmkd", table_c, values, precision=PRECISE)
    values = jnp.stack(turn(values, twiddle_c[0][None], twiddle_c[1][None]))
    parts = [
        jnp.einsum("qdk,qmcd->mck", table_d[p], values, precision=PRECISE)[None] for p in range(2)
    ]
    first = lax.broadcasted_iota(jnp.int32, (2, local_b, size_c, size_d), 0) == 0
    values = with_layout_constraint(jnp.where(first, *parts), Layout((0, 1, 2, 3)))
    return values.reshape(2, 1, 1, local_b, size_c, size_d)


def solution(mesh):
    return jax.shard_map(
        shards,
        mesh=mesh,
        in_specs=(P("wide", "narrow", None, None),),
        out_specs=P(None, "wide", "narrow", None, None, None),
        check_vma=False,
    )
```

```python
import math

import jax
import jax.numpy as jnp
from jax import lax
from jax.experimental.layout import Layout, with_layout_constraint
from jax.sharding import PartitionSpec as P

PRECISE = lax.Precision.HIGH
TWO_PI = 2.0 * math.pi
DEVICES = ("wide", "narrow")
LANES = 128


def reversed_digits(number, bit_count):
    result = 0 * number
    for position in range(bit_count):
        result = result + number // (1 << position) % 2 * (1 << bit_count - 1 - position)
    return result


def unit_turn(phases, length):
    angles = phases.astype(jnp.float32) * (TWO_PI / length)
    return jnp.cos(angles), jnp.sin(angles)


def block_table(inputs, outputs, length, factor):
    cosine, sines = unit_turn(inputs[:, None] * outputs[None, :] % length, length)
    cosine = cosine * factor
    sines = sines * factor
    return jnp.stack([jnp.stack([cosine, sines]), jnp.stack([-sines, cosine])])


def turn(values, cosine, sines):
    return values[0] * cosine + values[1] * sines, values[1] * cosine - values[0] * sines


def shards(record):
    local_a, local_b, size_c, size_d = record.shape
    wide_size = lax.axis_size("wide")
    narrow_size = lax.axis_size("narrow")
    levels = narrow_size.bit_length() - 1
    size_a = local_a * wide_size
    size_b = local_b * narrow_size
    total_count = size_a * size_b * size_c * size_d
    groups = wide_size * narrow_size
    column_count = local_b * size_c * size_d
    columns = column_count // groups
    here = lax.axis_index(DEVICES)

    gathered = lax.all_to_all(
        record.reshape(groups, columns), DEVICES, split_axis=0, concat_axis=0, tiled=True
    )
    slots = jnp.arange(groups, dtype=jnp.int32)
    frequency = slots // narrow_size + size_a * reversed_digits(slots % narrow_size, levels)
    cosine, sines = unit_turn(frequency[:, None] * slots[None, :] % groups, groups)
    scale = 1.0 / math.sqrt(total_count)
    table = jnp.concatenate([cosine * scale, -sines * scale])
    column_index = here * columns + jnp.arange(columns, dtype=jnp.int32)
    twiddle = unit_turn(frequency[:, None] * column_index[None, :] % total_count, total_count)
    gathered, table, twiddle = lax.optimization_barrier((gathered, table, twiddle))
    section = with_layout_constraint(
        jnp.dot(table, gathered, precision=PRECISE), Layout(major_to_minor=(0, 1))
    ).reshape(2, groups, columns)
    real, imag = (part[:, None] for part in turn(section, *twiddle))
    part_index = lax.broadcasted_iota(jnp.int32, (groups, 2, columns), 1)
    section = with_layout_constraint(jnp.where(part_index == 0, real, imag), Layout((0, 1, 2)))
    owned = lax.all_to_all(section, DEVICES, split_axis=0, concat_axis=0, tiled=True)

    index_b = jnp.arange(local_b, dtype=jnp.int32)
    table_b = block_table(index_b, index_b, local_b, 1.0)
    index_c = jnp.arange(size_c, dtype=jnp.int32)
    index_d = jnp.arange(size_d, dtype=jnp.int32)
    coarse = unit_turn(index_b[:, None] * (index_c * size_d)[None, :] % column_count, column_count)
    fine = unit_turn(index_b[:, None] * index_d[None, :] % column_count, column_count)
    table_c = block_table(index_c, index_c, size_c, 1.0)
    twiddle_c = unit_turn(index_c[:, None] * index_d[None, :] % (size_c * size_d), size_c * size_d)
    table_d = block_table(index_d, index_d, size_d, 1.0)
    owned, table_b, coarse, fine, table_c, twiddle_c, table_d = lax.optimization_barrier(
        (owned, table_b, coarse, fine, table_c, twiddle_c, table_d)
    )
    values = owned.reshape(local_b, groups // local_b, 2, columns)
    values = jnp.einsum("pqlm,lhqt->pmht", table_b, values, precision=PRECISE)
    values = values.reshape(2, local_b, size_c, size_d)
    cos_c, sin_c = coarse[0][:, :, None], coarse[1][:, :, None]
    cos_d, sin_d = fine[0][:, None, :], fine[1][:, None, :]
    twiddle_b = (cos_c * cos_d - sin_c * sin_d, sin_c * cos_d + cos_c * sin_d)
    values = jnp.stack(turn(values, *twiddle_b))
    values = jnp.einsum("pqck,qmcd->pmkd", table_c, values, precision=PRECISE)
    values = jnp.stack(turn(values, twiddle_c[0][None], twiddle_c[1][None]))
    values = jnp.einsum("pqdk,qmcd->pmck", table_d, values, precision=PRECISE)
    return values.reshape(2, 1, 1, local_b, size_c, size_d)


def solution(mesh):
    return jax.shard_map(
        shards,
        mesh=mesh,
        in_specs=(P("wide", "narrow", None, None),),
        out_specs=P(None, "wide", "narrow", None, None, None),
        check_vma=False,
    )
```

```python
import math

import jax
import jax.numpy as jnp
from jax import lax
from jax.experimental.layout import Layout, with_layout_constraint
from jax.sharding import PartitionSpec as P

PRECISE = lax.Precision.HIGH
TWO_PI = 2.0 * math.pi
DEVICES = ("wide", "narrow")
LANES = 128


def reversed_digits(number, bit_count):
    result = 0 * number
    for position in range(bit_count):
        result = result + number // (1 << position) % 2 * (1 << bit_count - 1 - position)
    return result


def unit_turn(phases, length):
    angles = phases.astype(jnp.float32) * (TWO_PI / length)
    return jnp.cos(angles), jnp.sin(angles)


def block_table(inputs, outputs, length, factor):
    cosine, sines = unit_turn(inputs[:, None] * outputs[None, :] % length, length)
    cosine = cosine * factor
    sines = sines * factor
    return jnp.stack([jnp.stack([cosine, sines]), jnp.stack([-sines, cosine])])


def turn(values, cosine, sines):
    return values[0] * cosine + values[1] * sines, values[1] * cosine - values[0] * sines


def shards(record):
    local_a, local_b, size_c, size_d = record.shape
    wide_size = lax.axis_size("wide")
    narrow_size = lax.axis_size("narrow")
    levels = narrow_size.bit_length() - 1
    size_a = local_a * wide_size
    size_b = local_b * narrow_size
    total_count = size_a * size_b * size_c * size_d
    groups = wide_size * narrow_size
    column_count = local_b * size_c * size_d
    columns = column_count // groups
    here = lax.axis_index(DEVICES)

    gathered = lax.all_to_all(
        record.reshape(groups, columns), DEVICES, split_axis=0, concat_axis=0, tiled=True
    )
    slots = jnp.arange(groups, dtype=jnp.int32)
    frequency = slots // narrow_size + size_a * reversed_digits(slots % narrow_size, levels)
    cosine, sines = unit_turn(frequency[:, None] * slots[None, :] % groups, groups)
    scale = 1.0 / math.sqrt(total_count)
    table = jnp.concatenate([cosine * scale, -sines * scale])
    column_index = here * columns + jnp.arange(columns, dtype=jnp.int32)
    twiddle = unit_turn(frequency[:, None] * column_index[None, :] % total_count, total_count)
    gathered, table, twiddle = lax.optimization_barrier((gathered, table, twiddle))
    section = with_layout_constraint(
        jnp.dot(table, gathered, precision=PRECISE), Layout(major_to_minor=(0, 1))
    ).reshape(2, groups, columns)
    real, imag = (part[:, None] for part in turn(section, *twiddle))
    part_index = lax.broadcasted_iota(jnp.int32, (groups, 2, columns), 1)
    section = with_layout_constraint(jnp.where(part_index == 0, real, imag), Layout((0, 1, 2)))
    owned = lax.all_to_all(section, DEVICES, split_axis=0, concat_axis=0, tiled=True)

    index_b = jnp.arange(local_b, dtype=jnp.int32)
    table_b = block_table(index_b, index_b, local_b, 1.0)
    inner = jnp.arange(size_c * size_d, dtype=jnp.int32)
    twiddle_b = unit_turn(index_b[:, None] * inner[None, :] % column_count, column_count)
    index_c = jnp.arange(size_c, dtype=jnp.int32)
    table_c = block_table(index_c, index_c, size_c, 1.0)
    index_d = jnp.arange(size_d, dtype=jnp.int32)
    twiddle_c = unit_turn(index_c[:, None] * index_d[None, :] % (size_c * size_d), size_c * size_d)
    table_d = block_table(index_d, index_d, size_d, 1.0)
    owned, table_b, twiddle_b, table_c, twiddle_c, table_d = lax.optimization_barrier(
        (owned, table_b, twiddle_b, table_c, twiddle_c, table_d)
    )
    values = owned.reshape(local_b, groups // local_b, 2, columns)
    values = jnp.einsum("pqlm,lhqt->pmht", table_b, values, precision=PRECISE)
    values = values.reshape(2, local_b, size_c * size_d)
    values = jnp.stack(turn(values, *twiddle_b)).reshape(2, local_b, size_c, size_d)
    values = jnp.einsum("pqck,qmcd->pmkd", table_c, values, precision=PRECISE)
    values = jnp.stack(turn(values, twiddle_c[0][None], twiddle_c[1][None]))
    values = jnp.einsum("qmcd,pqdk->pmck", values, table_d, precision=PRECISE)
    return values.reshape(2, 1, 1, local_b, size_c, size_d)


def solution(mesh):
    return jax.shard_map(
        shards,
        mesh=mesh,
        in_specs=(P("wide", "narrow", None, None),),
        out_specs=P(None, "wide", "narrow", None, None, None),
        check_vma=False,
    )
```

```python
import math

import jax
import jax.numpy as jnp
from jax import lax
from jax.experimental.layout import Layout, with_layout_constraint
from jax.sharding import PartitionSpec as P

PRECISE = lax.Precision.HIGH
TWO_PI = 2.0 * math.pi
DEVICES = ("wide", "narrow")
LANES = 128


def reversed_digits(number, bit_count):
    result = 0 * number
    for position in range(bit_count):
        result = result + number // (1 << position) % 2 * (1 << bit_count - 1 - position)
    return result


def unit_turn(phases, length):
    angles = phases.astype(jnp.float32) * (TWO_PI / length)
    return jnp.cos(angles), jnp.sin(angles)


def block_table(inputs, outputs, length, factor):
    cosine, sines = unit_turn(inputs[:, None] * outputs[None, :] % length, length)
    cosine = cosine * factor
    sines = sines * factor
    return jnp.stack([jnp.stack([cosine, sines]), jnp.stack([-sines, cosine])])


def turn(values, cosine, sines):
    return values[0] * cosine + values[1] * sines, values[1] * cosine - values[0] * sines


def shards(record):
    local_a, local_b, size_c, size_d = record.shape
    wide_size = lax.axis_size("wide")
    narrow_size = lax.axis_size("narrow")
    levels = narrow_size.bit_length() - 1
    size_a = local_a * wide_size
    size_b = local_b * narrow_size
    total_count = size_a * size_b * size_c * size_d
    groups = wide_size * narrow_size
    column_count = local_b * size_c * size_d
    columns = column_count // groups
    here = lax.axis_index(DEVICES)

    gathered = lax.all_to_all(
        record.reshape(groups, columns), DEVICES, split_axis=0, concat_axis=0, tiled=True
    )
    slots = jnp.arange(groups, dtype=jnp.int32)
    frequency = slots // narrow_size + size_a * reversed_digits(slots % narrow_size, levels)
    cosine, sines = unit_turn(frequency[:, None] * slots[None, :] % groups, groups)
    scale = 1.0 / math.sqrt(total_count)
    table = jnp.concatenate([cosine * scale, -sines * scale])
    column_index = here * columns + jnp.arange(columns, dtype=jnp.int32)
    twiddle = unit_turn(frequency[:, None] * column_index[None, :] % total_count, total_count)
    gathered, table, twiddle = lax.optimization_barrier((gathered, table, twiddle))
    section = with_layout_constraint(
        jnp.dot(table, gathered, precision=PRECISE), Layout(major_to_minor=(0, 1))
    ).reshape(2, groups, columns)
    real, imag = (part[:, None] for part in turn(section, *twiddle))
    part_index = lax.broadcasted_iota(jnp.int32, (groups, 2, columns), 1)
    section = with_layout_constraint(jnp.where(part_index == 0, real, imag), Layout((0, 1, 2)))
    owned = lax.all_to_all(section, DEVICES, split_axis=0, concat_axis=0, tiled=True)

    index_b = jnp.arange(local_b, dtype=jnp.int32)
    table_b = block_table(index_b, index_b, local_b, 1.0)
    inner = jnp.arange(size_c * size_d, dtype=jnp.int32)
    twiddle_b = unit_turn(index_b[:, None] * inner[None, :] % column_count, column_count)
    index_c = jnp.arange(size_c, dtype=jnp.int32)
    table_c = block_table(index_c, index_c, size_c, 1.0)
    index_d = jnp.arange(size_d, dtype=jnp.int32)
    twiddle_c = unit_turn(index_c[:, None] * index_d[None, :] % (size_c * size_d), size_c * size_d)
    table_d = block_table(index_d, index_d, size_d, 1.0)
    owned, table_b, twiddle_b, table_c, twiddle_c, table_d = lax.optimization_barrier(
        (owned, table_b, twiddle_b, table_c, twiddle_c, table_d)
    )
    values = owned.reshape(local_b, groups // local_b, 2, columns)
    values = jnp.einsum("pqlm,lhqt->pmht", table_b, values, precision=PRECISE)
    values = values.reshape(2, local_b, size_c * size_d)
    values = jnp.stack(turn(values, *twiddle_b)).reshape(2, local_b, size_c, size_d)
    values = jnp.einsum("qmcd,pqck->pmkd", values, table_c, precision=PRECISE)
    values = jnp.stack(turn(values, twiddle_c[0][None], twiddle_c[1][None]))
    values = jnp.einsum("qmcd,pqdk->pmck", values, table_d, precision=PRECISE)
    return values.reshape(2, 1, 1, local_b, size_c, size_d)


def solution(mesh):
    return jax.shard_map(
        shards,
        mesh=mesh,
        in_specs=(P("wide", "narrow", None, None),),
        out_specs=P(None, "wide", "narrow", None, None, None),
        check_vma=False,
    )
```
